512 devices in a mesh: walker: 32 (over z, y_lo), orb: 16 (over x, y_hi, core).
Axes of the slice: x: 4, y: 4 (y_hi: 2, y_lo: 2; y = y_hi * 2 + y_lo), z: 16, core: 2. Of those that a mesh axis runs over, the one named last changes fastest.
Arguments:
- tile_index: int32 [32768], P('walker'), may hold values from 0 to 63
- weights: bfloat16 [32768, 64], P('walker'), may hold values from -0.75 to 0.75
- electron: int32 [32768], P('walker'), may hold values from 0 to 767
- strength: float32 [32768], P('walker'), may hold values from -1.5 to 1.5
- spline_table: bfloat16 [4096, 4096], P(None, 'orb'), may hold values from -6 to 6
- rotation: bfloat16 [4096, 768], P('orb'), may hold values from -0.09375 to 0.09375
- inverse: bfloat16 [32, 768, 768], P('walker', 'orb'), may hold values from -0.21875 to 0.21875
Outputs:
- ratios: float32 [32768], P(('walker', 'orb'))
- gradient: float32 [4096, 768], P('orb')
The draws below stay inside these ranges and needn't reach their ends.
All inputs are finite; a program needn't handle non-finite values.
Results may differ from the reference program's by a relative error of at most 0.0042.
Values may be sent and summed in bfloat16 or wider, within the bound.
No kernel may reach another device: no remote copies, remote signals or barrier semaphores. Data moves between devices by JAX's collectives and lax.ppermute only.
A program may use at most 64 MiB of HBM per device.

```python
import jax
import jax.numpy as jnp
from jax import lax

ELECTRONS = 768
ORBITALS = 4096
COEFFS = 64
TILES = 64
PTS_W = 1024
WALKERS = 32
PTS = 32768
ROWS = 4096
N_WALKER = 32


def with_ends(drawn, rng, least, largest):
    spot = [jax.random.randint(jax.random.fold_in(rng, axis), (), 0, length) for axis, length in enumerate(drawn.shape)]
    main_axis = drawn.shape.index(max(drawn.shape))
    next_to = spot[:main_axis] + [(spot[main_axis] + 1) % drawn.shape[main_axis]] + spot[main_axis + 1:]
    return drawn.at[tuple(spot)].set(least).at[tuple(next_to)].set(largest)


def level_of(key, shape, cuts, least, top_value):
    def one(dim, shards_of):
        draws = jax.random.uniform(jax.random.fold_in(jax.random.fold_in(key, 6), dim), (shards_of,), jnp.float32, least / len(cuts), top_value / len(cuts))
        return jnp.repeat(jnp.exp(draws), shape[dim] // shards_of).reshape((-1,) + (1,) * (len(shape) - dim - 1))

    gain = one(*cuts[0])
    for cut in cuts[1:]:
        gain = gain * one(*cut)
    return gain


def bell_draw(stream_key, dims, spread, reach, pieces=(), dtype=jnp.bfloat16):
    level = level_of(stream_key, dims, pieces, -0.22, 0.18) if pieces else 1.0
    array = jax.random.normal(stream_key, dims, jnp.float32) * spread * level
    return jnp.minimum(jnp.maximum(array, -reach), reach).astype(dtype)


def setup_inputs(seed: int = 0) -> dict:
    keys = jax.random.split(jax.random.key(seed), 8)
    return {
        "tile_index": with_ends(jax.random.randint(keys[0], (PTS,), 0, TILES), jax.random.fold_in(keys[0], 1), 0, TILES - 1).astype(jnp.int32),
        "weights": bell_draw(keys[1], (PTS, COEFFS), 0.125, 0.75, ((0, 32),)),
        "electron": with_ends(jax.random.randint(keys[2], (PTS,), 0, ELECTRONS), jax.random.fold_in(keys[2], 1), 0, ELECTRONS - 1).astype(jnp.int32),
        "strength": bell_draw(keys[3], (PTS,), 0.25, 1.5, ((0, 32),), jnp.float32),
        "spline_table": bell_draw(keys[4], (ROWS, ORBITALS), 1.0, 6.0, ((1, 16),)),
        "rotation": bell_draw(keys[5], (ORBITALS, ELECTRONS), ORBITALS ** -0.5, 0.09375, ((0, 16),)),
        "inverse": bell_draw(keys[6], (WALKERS, ELECTRONS, ELECTRONS), ELECTRONS ** -0.5, 0.21875, ((0, 32), (1, 16))),
    }


def spline_values(tiles, coeffs, grid):
    def block_values(items):
        tile_block, coeff_block = items
        rows_found = grid[tile_block].astype(jnp.float32)
        return jnp.einsum("pk,pkm->pm", coeff_block.astype(jnp.float32), rows_found).astype(jnp.bfloat16)
    blocks = lax.map(block_values, (tiles.reshape(-1, 64), coeffs.reshape(-1, 64, COEFFS)))
    return blocks.reshape(tiles.shape[0], ORBITALS)


def reference(tile_index, weights, electron, strength, spline_table, rotation, inverse):
    grid = spline_table.reshape(TILES, COEFFS, ORBITALS)
    rotation_wide = rotation.astype(jnp.float32)

    def walker_step(total, items):
        tiles, coeffs, owners, potential, inverse_walker = items
        orbital_values = spline_values(tiles, coeffs, grid)
        values_wide = orbital_values.astype(jnp.float32)
        rotated = jnp.dot(values_wide, rotation_wide, preferred_element_type=jnp.float32)
        columns = jnp.take(inverse_walker, owners, axis=1).astype(jnp.float32)
        ratio = jnp.sum(rotated.T * columns, axis=0)
        adjoint = (columns * potential[None, :]).astype(jnp.bfloat16)
        adjoint_wide = adjoint.astype(jnp.float32)
        total = total + jnp.dot(values_wide.T, adjoint_wide.T, preferred_element_type=jnp.float32)
        return total, ratio

    start_total = jnp.zeros((ORBITALS, ELECTRONS), jnp.float32)
    total, ratios = lax.scan(walker_step, start_total, (tile_index.reshape(N_WALKER, PTS_W), weights.reshape(N_WALKER, PTS_W, COEFFS), electron.reshape(N_WALKER, PTS_W), strength.reshape(N_WALKER, PTS_W), inverse))
    return ratios.reshape(-1), total
```

```python
import jax
import jax.numpy as jnp
from jax import lax
from jax.sharding import PartitionSpec as P


def body(tile_index, weights, electron, strength, spline_table, rotation, inverse):
    points = tile_index.shape[0]
    coeffs = weights.shape[1]
    tiles_count = spline_table.shape[0] // coeffs
    electrons = inverse.shape[2]
    inverse_full = lax.all_gather(inverse[0], "orb", axis=0, tiled=True)
    onehot = (tile_index[:, None] == jnp.arange(tiles_count, dtype=jnp.int32)[None, :]).astype(
        jnp.bfloat16
    )
    stencil_matrix = (onehot[:, :, None] * weights[:, None, :]).reshape(
        points, tiles_count * coeffs
    )
    orbital_values = jnp.dot(
        stencil_matrix, spline_table, preferred_element_type=jnp.float32
    ).astype(jnp.bfloat16)
    pick = (electron[:, None] == jnp.arange(electrons, dtype=jnp.int32)[None, :]).astype(
        jnp.bfloat16
    )
    columns = lax.dot_general(
        pick, inverse_full, (((1,), (1,)), ((), ())), preferred_element_type=jnp.float32
    )
    adjoint = (columns * strength[:, None]).astype(jnp.bfloat16)
    local_gradient = lax.dot_general(
        orbital_values, adjoint, (((0,), (0,)), ((), ())), preferred_element_type=jnp.float32
    )
    rotated_columns = lax.dot_general(
        columns.astype(jnp.bfloat16),
        rotation,
        (((1,), (1,)), ((), ())),
        preferred_element_type=jnp.float32,
    )
    partial_ratio = jnp.sum(orbital_values.astype(jnp.float32) * rotated_columns, axis=1)
    ratios = lax.psum_scatter(partial_ratio, "orb", scatter_dimension=0, tiled=True)
    gradient = lax.psum(local_gradient, "walker")
    return (ratios, gradient)


def solution(mesh):
    in_specs = (
        P("walker"),
        P("walker", None),
        P("walker"),
        P("walker"),
        P(None, "orb"),
        P("orb", None),
        P("walker", "orb", None),
    )
    out_specs = (P(("walker", "orb")), P("orb", None))
    return jax.shard_map(body, mesh=mesh, in_specs=in_specs, out_specs=out_specs, check_vma=False)
```

```python
import jax
import jax.numpy as jnp
from jax import lax
from jax.sharding import PartitionSpec as P


def _bits(axis):
    size = lax.axis_size(axis)
    count = size.bit_length() - 1
    assert 1 << count == size
    return size, count


def _exchange(x, axis, size, bit):
    pairs = [(i, i ^ (1 << bit)) for i in range(size)]
    return lax.ppermute(x, axis, pairs)


def _pick(x, which):
    return lax.dynamic_index_in_dim(x, which, 0, keepdims=False)


def reduce_scatter_bits(x, axis, order):
    size, _ = _bits(axis)
    me = lax.axis_index(axis)
    for bit in order:
        mine = (me >> bit) & 1
        keep = _pick(x, mine)
        send = _pick(x, 1 - mine)
        x = keep + _exchange(send, axis, size, bit)
    return x


def all_gather_bits(x, axis, order):
    size, _ = _bits(axis)
    me = lax.axis_index(axis)
    for bit in order:
        mine = (me >> bit) & 1
        other = _exchange(x, axis, size, bit)
        x = jnp.where(mine == 0, jnp.stack([x, other]), jnp.stack([other, x]))
    return x


def all_reduce_bits(x, axis):
    size, count = _bits(axis)
    tail = x.shape
    rows = tail[0] >> count
    parts = x.reshape((2,) * count + (rows,) + tail[1:])
    order = list(range(count))
    reduced = reduce_scatter_bits(parts, axis, order)
    return all_gather_bits(reduced, axis, order[::-1]).reshape(tail)


def body(tile_index, weights, electron, strength, spline_table, rotation, inverse):
    points = tile_index.shape[0]
    coeffs = weights.shape[1]
    tiles_count = spline_table.shape[0] // coeffs
    electrons = inverse.shape[2]
    _, orb_bits = _bits("orb")
    inverse_full = all_gather_bits(inverse[0], "orb", list(range(orb_bits)))
    inverse_full = inverse_full.reshape(-1, electrons)
    onehot = (tile_index[:, None] == jnp.arange(tiles_count, dtype=jnp.int32)[None, :]).astype(
        jnp.bfloat16
    )
    stencil_matrix = (onehot[:, :, None] * weights[:, None, :]).reshape(
        points, tiles_count * coeffs
    )
    orbital_values = jnp.dot(
        stencil_matrix, spline_table, preferred_element_type=jnp.float32
    ).astype(jnp.bfloat16)
    pick = (electron[:, None] == jnp.arange(electrons, dtype=jnp.int32)[None, :]).astype(
        jnp.bfloat16
    )
    columns = lax.dot_general(
        pick, inverse_full, (((1,), (1,)), ((), ())), preferred_element_type=jnp.float32
    )
    adjoint = (columns * strength[:, None]).astype(jnp.bfloat16)
    local_gradient = lax.dot_general(
        orbital_values, adjoint, (((0,), (0,)), ((), ())), preferred_element_type=jnp.float32
    )
    rotated_columns = lax.dot_general(
        columns.astype(jnp.bfloat16),
        rotation,
        (((1,), (1,)), ((), ())),
        preferred_element_type=jnp.float32,
    )
    partial_ratio = jnp.sum(orbital_values.astype(jnp.float32) * rotated_columns, axis=1)
    share = points >> orb_bits
    ratio_parts = partial_ratio.reshape((2,) * orb_bits + (share,))
    ratios = reduce_scatter_bits(ratio_parts, "orb", list(range(orb_bits - 1, -1, -1)))
    gradient = all_reduce_bits(local_gradient, "walker")
    return (ratios, gradient)


def solution(mesh):
    in_specs = (
        P("walker"),
        P("walker", None),
        P("walker"),
        P("walker"),
        P(None, "orb"),
        P("orb", None),
        P("walker", "orb", None),
    )
    out_specs = (P(("walker", "orb")), P("orb", None))
    return jax.shard_map(body, mesh=mesh, in_specs=in_specs, out_specs=out_specs, check_vma=False)
```

```python
import jax
import jax.numpy as jnp
from jax import lax
from jax.sharding import PartitionSpec as P


def _bits(axis):
    size = lax.axis_size(axis)
    count = size.bit_length() - 1
    assert 1 << count == size
    return size, count


def _exchange(x, axis, size, bit):
    pairs = [(i, i ^ (1 << bit)) for i in range(size)]
    return lax.ppermute(x, axis, pairs)


def _pick(x, which):
    return lax.dynamic_index_in_dim(x, which, 0, keepdims=False)


def reduce_scatter_bits(x, axis, order):
    size, _ = _bits(axis)
    me = lax.axis_index(axis)
    for bit in order:
        mine = (me >> bit) & 1
        keep = _pick(x, mine)
        send = _pick(x, 1 - mine)
        x = keep + _exchange(send, axis, size, bit)
    return x


def all_gather_bits(x, axis, order):
    size, _ = _bits(axis)
    me = lax.axis_index(axis)
    for bit in order:
        mine = (me >> bit) & 1
        other = _exchange(x, axis, size, bit)
        x = jnp.where(mine == 0, jnp.stack([x, other]), jnp.stack([other, x]))
    return x


def all_reduce_bits(x, axis):
    size, count = _bits(axis)
    tail = x.shape
    rows = tail[0] >> count
    parts = x.reshape((2,) * count + (rows,) + tail[1:])
    order = list(range(count))
    reduced = reduce_scatter_bits(parts, axis, order)
    return all_gather_bits(reduced, axis, order[::-1]).reshape(tail)


def gather_by_all_to_all(x, axis):
    size = lax.axis_size(axis)
    copies = jnp.broadcast_to(x[None], (size,) + x.shape)
    return lax.all_to_all(copies, axis, 0, 0, tiled=True)


def reduce_scatter_by_all_to_all(x, axis):
    size = lax.axis_size(axis)
    parts = x.reshape((size, x.shape[0] // size) + x.shape[1:])
    return jnp.sum(lax.all_to_all(parts, axis, 0, 0, tiled=True), axis=0)


def body(tile_index, weights, electron, strength, spline_table, rotation, inverse):
    points = tile_index.shape[0]
    coeffs = weights.shape[1]
    tiles_count = spline_table.shape[0] // coeffs
    electrons = inverse.shape[2]
    _, orb_bits = _bits("orb")
    inverse_full = gather_by_all_to_all(inverse[0], "orb").reshape(-1, electrons)
    onehot = (tile_index[:, None] == jnp.arange(tiles_count, dtype=jnp.int32)[None, :]).astype(
        jnp.bfloat16
    )
    stencil_matrix = (onehot[:, :, None] * weights[:, None, :]).reshape(
        points, tiles_count * coeffs
    )
    orbital_values = jnp.dot(
        stencil_matrix, spline_table, preferred_element_type=jnp.float32
    ).astype(jnp.bfloat16)
    pick = (electron[:, None] == jnp.arange(electrons, dtype=jnp.int32)[None, :]).astype(
        jnp.bfloat16
    )
    columns = lax.dot_general(
        pick, inverse_full, (((1,), (1,)), ((), ())), preferred_element_type=jnp.float32
    )
    adjoint = (columns * strength[:, None]).astype(jnp.bfloat16)
    local_gradient = lax.dot_general(
        orbital_values, adjoint, (((0,), (0,)), ((), ())), preferred_element_type=jnp.float32
    )
    rotated_columns = lax.dot_general(
        columns.astype(jnp.bfloat16),
        rotation,
        (((1,), (1,)), ((), ())),
        preferred_element_type=jnp.float32,
    )
    partial_ratio = jnp.sum(orbital_values.astype(jnp.float32) * rotated_columns, axis=1)
    ratios = reduce_scatter_by_all_to_all(partial_ratio, "orb")
    reduced = reduce_scatter_by_all_to_all(local_gradient, "walker")
    gradient = gather_by_all_to_all(reduced, "walker").reshape(local_gradient.shape)
    return (ratios, gradient)


def solution(mesh):
    in_specs = (
        P("walker"),
        P("walker", None),
        P("walker"),
        P("walker"),
        P(None, "orb"),
        P("orb", None),
        P("walker", "orb", None),
    )
    out_specs = (P(("walker", "orb")), P("orb", None))
    return jax.shard_map(body, mesh=mesh, in_specs=in_specs, out_specs=out_specs, check_vma=False)
```

```python
import jax
import jax.numpy as jnp
from jax import lax
from jax.sharding import Mesh, PartitionSpec as P


def _bits(axis):
    size = lax.axis_size(axis)
    count = size.bit_length() - 1
    assert 1 << count == size
    return size, count


def _exchange(x, axis, size, bit):
    pairs = [(i, i ^ (1 << bit)) for i in range(size)]
    return lax.ppermute(x, axis, pairs)


def _pick(x, which):
    return lax.dynamic_index_in_dim(x, which, 0, keepdims=False)


def reduce_scatter_bits(x, axis, order):
    size, _ = _bits(axis)
    me = lax.axis_index(axis)
    for bit in order:
        mine = (me >> bit) & 1
        keep = _pick(x, mine)
        send = _pick(x, 1 - mine)
        x = keep + _exchange(send, axis, size, bit)
    return x


def all_gather_bits(x, axis, order):
    size, _ = _bits(axis)
    me = lax.axis_index(axis)
    for bit in order:
        mine = (me >> bit) & 1
        other = _exchange(x, axis, size, bit)
        x = jnp.where(mine == 0, jnp.stack([x, other]), jnp.stack([other, x]))
    return x


def all_reduce_bits(x, axis):
    size, count = _bits(axis)
    tail = x.shape
    rows = tail[0] >> count
    parts = x.reshape((2,) * count + (rows,) + tail[1:])
    order = list(range(count))
    reduced = reduce_scatter_bits(parts, axis, order)
    return all_gather_bits(reduced, axis, order[::-1]).reshape(tail)


def all_reduce_walker(x):
    me = lax.axis_index("wy")
    halves = x.reshape((2, x.shape[0] // 2) + x.shape[1:])
    keep = _pick(halves, me)
    half = keep + lax.ppermute(_pick(halves, 1 - me), "wy", [(0, 1), (1, 0)])
    reduced = reduce_scatter_by_all_to_all(half, "wz")
    half = gather_by_all_to_all(reduced, "wz").reshape(half.shape)
    other = lax.ppermute(half, "wy", [(0, 1), (1, 0)])
    return jnp.where(me == 0, jnp.stack([half, other]), jnp.stack([other, half])).reshape(x.shape)


def gather_by_all_to_all(x, axis):
    size = lax.axis_size(axis)
    copies = jnp.broadcast_to(x[None], (size,) + x.shape)
    return lax.all_to_all(copies, axis, 0, 0, tiled=True)


def reduce_scatter_by_all_to_all(x, axis):
    size = lax.axis_size(axis)
    parts = x.reshape((size, x.shape[0] // size) + x.shape[1:])
    return jnp.sum(lax.all_to_all(parts, axis, 0, 0, tiled=True), axis=0)


def body(tile_index, weights, electron, strength, spline_table, rotation, inverse):
    points = tile_index.shape[0]
    coeffs = weights.shape[1]
    tiles_count = spline_table.shape[0] // coeffs
    electrons = inverse.shape[2]
    _, orb_bits = _bits("orb")
    inverse_full = gather_by_all_to_all(inverse[0], "orb").reshape(-1, electrons)
    onehot = (tile_index[:, None] == jnp.arange(tiles_count, dtype=jnp.int32)[None, :]).astype(
        jnp.bfloat16
    )
    stencil_matrix = (onehot[:, :, None] * weights[:, None, :]).reshape(
        points, tiles_count * coeffs
    )
    orbital_values = jnp.dot(
        stencil_matrix, spline_table, preferred_element_type=jnp.float32
    ).astype(jnp.bfloat16)
    pick = (electron[:, None] == jnp.arange(electrons, dtype=jnp.int32)[None, :]).astype(
        jnp.bfloat16
    )
    columns = lax.dot_general(
        pick, inverse_full, (((1,), (1,)), ((), ())), preferred_element_type=jnp.float32
    )
    adjoint = (columns * strength[:, None]).astype(jnp.bfloat16)
    local_gradient = lax.dot_general(
        orbital_values, adjoint, (((0,), (0,)), ((), ())), preferred_element_type=jnp.float32
    )
    rotated_columns = lax.dot_general(
        columns.astype(jnp.bfloat16),
        rotation,
        (((1,), (1,)), ((), ())),
        preferred_element_type=jnp.float32,
    )
    partial_ratio = jnp.sum(orbital_values.astype(jnp.float32) * rotated_columns, axis=1)
    ratios = reduce_scatter_by_all_to_all(partial_ratio, "orb")
    gradient = all_reduce_walker(local_gradient)
    return (ratios, gradient)


def solution(mesh):
    sizes = dict(mesh.shape)
    split = Mesh(
        mesh.devices.reshape(sizes["walker"] // 2, 2, sizes["orb"]), ("wz", "wy", "orb")
    )
    walker = ("wz", "wy")
    in_specs = (
        P(walker),
        P(walker, None),
        P(walker),
        P(walker),
        P(None, "orb"),
        P("orb", None),
        P(walker, "orb", None),
    )
    out_specs = (P(walker + ("orb",)), P("orb", None))
    return jax.shard_map(body, mesh=split, in_specs=in_specs, out_specs=out_specs, check_vma=False)
```

```python
import jax
import jax.numpy as jnp
from jax import lax
from jax.sharding import Mesh, PartitionSpec as P


def _bits(axis):
    size = lax.axis_size(axis)
    count = size.bit_length() - 1
    assert 1 << count == size
    return size, count


def _exchange(x, axis, size, bit):
    pairs = [(i, i ^ (1 << bit)) for i in range(size)]
    return lax.ppermute(x, axis, pairs)


def _pick(x, which):
    return lax.dynamic_index_in_dim(x, which, 0, keepdims=False)


def reduce_scatter_bits(x, axis, order):
    size, _ = _bits(axis)
    me = lax.axis_index(axis)
    for bit in order:
        mine = (me >> bit) & 1
        keep = _pick(x, mine)
        send = _pick(x, 1 - mine)
        x = keep + _exchange(send, axis, size, bit)
    return x


def all_gather_bits(x, axis, order):
    size, _ = _bits(axis)
    me = lax.axis_index(axis)
    for bit in order:
        mine = (me >> bit) & 1
        other = _exchange(x, axis, size, bit)
        x = jnp.where(mine == 0, jnp.stack([x, other]), jnp.stack([other, x]))
    return x


def all_reduce_bits(x, axis):
    size, count = _bits(axis)
    tail = x.shape
    rows = tail[0] >> count
    parts = x.reshape((2,) * count + (rows,) + tail[1:])
    order = list(range(count))
    reduced = reduce_scatter_bits(parts, axis, order)
    return all_gather_bits(reduced, axis, order[::-1]).reshape(tail)


def all_reduce_walker(x, rider):
    me = lax.axis_index("wy")
    halves = x.reshape((2, x.shape[0] // 2) + x.shape[1:])
    keep = _pick(halves, me)
    half = keep + lax.ppermute(_pick(halves, 1 - me), "wy", [(0, 1), (1, 0)])
    half, rider = lax.optimization_barrier((half, rider))
    reduced = reduce_scatter_by_all_to_all(half, "wz")
    half = gather_by_all_to_all(reduced, "wz").reshape(half.shape)
    other = lax.ppermute(half, "wy", [(0, 1), (1, 0)])
    full = jnp.where(me == 0, jnp.stack([half, other]), jnp.stack([other, half]))
    return full.reshape(x.shape), rider


def gather_by_all_to_all(x, axis):
    size = lax.axis_size(axis)
    copies = jnp.broadcast_to(x[None], (size,) + x.shape)
    return lax.all_to_all(copies, axis, 0, 0, tiled=True)


def reduce_scatter_by_all_to_all(x, axis):
    size = lax.axis_size(axis)
    parts = x.reshape((size, x.shape[0] // size) + x.shape[1:])
    return jnp.sum(lax.all_to_all(parts, axis, 0, 0, tiled=True), axis=0)


def body(tile_index, weights, electron, strength, spline_table, rotation, inverse):
    points = tile_index.shape[0]
    coeffs = weights.shape[1]
    tiles_count = spline_table.shape[0] // coeffs
    electrons = inverse.shape[2]
    _, orb_bits = _bits("orb")
    inverse_full = gather_by_all_to_all(inverse[0], "orb").reshape(-1, electrons)
    onehot = (tile_index[:, None] == jnp.arange(tiles_count, dtype=jnp.int32)[None, :]).astype(
        jnp.bfloat16
    )
    stencil_matrix = (onehot[:, :, None] * weights[:, None, :]).reshape(
        points, tiles_count * coeffs
    )
    orbital_values = jnp.dot(
        stencil_matrix, spline_table, preferred_element_type=jnp.float32
    ).astype(jnp.bfloat16)
    pick = (electron[:, None] == jnp.arange(electrons, dtype=jnp.int32)[None, :]).astype(
        jnp.bfloat16
    )
    columns = lax.dot_general(
        pick, inverse_full, (((1,), (1,)), ((), ())), preferred_element_type=jnp.float32
    )
    adjoint = (columns * strength[:, None]).astype(jnp.bfloat16)
    local_gradient = lax.dot_general(
        orbital_values, adjoint, (((0,), (0,)), ((), ())), preferred_element_type=jnp.float32
    )
    rotated_columns = lax.dot_general(
        columns.astype(jnp.bfloat16),
        rotation,
        (((1,), (1,)), ((), ())),
        preferred_element_type=jnp.float32,
    )
    partial_ratio = jnp.sum(orbital_values.astype(jnp.float32) * rotated_columns, axis=1)
    ratios = reduce_scatter_by_all_to_all(partial_ratio, "orb")
    gradient, ratios = all_reduce_walker(local_gradient, ratios)
    return (ratios, gradient)


def solution(mesh):
    sizes = dict(mesh.shape)
    split = Mesh(
        mesh.devices.reshape(sizes["walker"] // 2, 2, sizes["orb"]), ("wz", "wy", "orb")
    )
    walker = ("wz", "wy")
    in_specs = (
        P(walker),
        P(walker, None),
        P(walker),
        P(walker),
        P(None, "orb"),
        P("orb", None),
        P(walker, "orb", None),
    )
    out_specs = (P(walker + ("orb",)), P("orb", None))
    return jax.shard_map(body, mesh=split, in_specs=in_specs, out_specs=out_specs, check_vma=False)
```

```python
import jax
import jax.numpy as jnp
from jax import lax
from jax.sharding import Mesh, PartitionSpec as P


def _bits(axis):
    size = lax.axis_size(axis)
    count = size.bit_length() - 1
    assert 1 << count == size
    return size, count


def _exchange(x, axis, size, bit):
    pairs = [(i, i ^ (1 << bit)) for i in range(size)]
    return lax.ppermute(x, axis, pairs)


def _pick(x, which):
    return lax.dynamic_index_in_dim(x, which, 0, keepdims=False)


def reduce_scatter_bits(x, axis, order):
    size, _ = _bits(axis)
    me = lax.axis_index(axis)
    for bit in order:
        mine = (me >> bit) & 1
        keep = _pick(x, mine)
        send = _pick(x, 1 - mine)
        x = keep + _exchange(send, axis, size, bit)
    return x


def all_gather_bits(x, axis, order):
    size, _ = _bits(axis)
    me = lax.axis_index(axis)
    for bit in order:
        mine = (me >> bit) & 1
        other = _exchange(x, axis, size, bit)
        x = jnp.where(mine == 0, jnp.stack([x, other]), jnp.stack([other, x]))
    return x


def all_reduce_bits(x, axis):
    size, count = _bits(axis)
    tail = x.shape
    rows = tail[0] >> count
    parts = x.reshape((2,) * count + (rows,) + tail[1:])
    order = list(range(count))
    reduced = reduce_scatter_bits(parts, axis, order)
    return all_gather_bits(reduced, axis, order[::-1]).reshape(tail)


def all_reduce_walker(x, rider):
    me = lax.axis_index("wy")
    halves = x.reshape((2, x.shape[0] // 2) + x.shape[1:])
    keep = _pick(halves, me)
    half = keep + lax.ppermute(_pick(halves, 1 - me), "wy", [(0, 1), (1, 0)])
    half, rider = lax.optimization_barrier((half, rider))
    reduced = reduce_scatter_by_all_to_all(half, "wz").astype(jnp.bfloat16)
    half = gather_by_all_to_all(reduced, "wz").reshape(half.shape)
    other = lax.ppermute(half, "wy", [(0, 1), (1, 0)])
    full = jnp.where(me == 0, jnp.stack([half, other]), jnp.stack([other, half]))
    return full.reshape(x.shape).astype(x.dtype), rider


def gather_by_all_to_all(x, axis):
    size = lax.axis_size(axis)
    copies = jnp.broadcast_to(x[None], (size,) + x.shape)
    return lax.all_to_all(copies, axis, 0, 0, tiled=True)


def reduce_scatter_by_all_to_all(x, axis):
    size = lax.axis_size(axis)
    parts = x.reshape((size, x.shape[0] // size) + x.shape[1:])
    return jnp.sum(lax.all_to_all(parts, axis, 0, 0, tiled=True), axis=0)


def body(tile_index, weights, electron, strength, spline_table, rotation, inverse):
    points = tile_index.shape[0]
    coeffs = weights.shape[1]
    tiles_count = spline_table.shape[0] // coeffs
    electrons = inverse.shape[2]
    _, orb_bits = _bits("orb")
    inverse_full = gather_by_all_to_all(inverse[0], "orb").reshape(-1, electrons)
    onehot = (tile_index[:, None] == jnp.arange(tiles_count, dtype=jnp.int32)[None, :]).astype(
        jnp.bfloat16
    )
    stencil_matrix = (onehot[:, :, None] * weights[:, None, :]).reshape(
        points, tiles_count * coeffs
    )
    orbital_values = jnp.dot(
        stencil_matrix, spline_table, preferred_element_type=jnp.float32
    ).astype(jnp.bfloat16)
    pick = (electron[:, None] == jnp.arange(electrons, dtype=jnp.int32)[None, :]).astype(
        jnp.bfloat16
    )
    columns = lax.dot_general(
        pick, inverse_full, (((1,), (1,)), ((), ())), preferred_element_type=jnp.float32
    )
    adjoint = (columns * strength[:, None]).astype(jnp.bfloat16)
    local_gradient = lax.dot_general(
        orbital_values, adjoint, (((0,), (0,)), ((), ())), preferred_element_type=jnp.float32
    )
    rotated_columns = lax.dot_general(
        columns.astype(jnp.bfloat16),
        rotation,
        (((1,), (1,)), ((), ())),
        preferred_element_type=jnp.float32,
    )
    partial_ratio = jnp.sum(orbital_values.astype(jnp.float32) * rotated_columns, axis=1)
    ratios = reduce_scatter_by_all_to_all(partial_ratio, "orb")
    gradient, ratios = all_reduce_walker(local_gradient, ratios)
    return (ratios, gradient)


def solution(mesh):
    sizes = dict(mesh.shape)
    split = Mesh(
        mesh.devices.reshape(sizes["walker"] // 2, 2, sizes["orb"]), ("wz", "wy", "orb")
    )
    walker = ("wz", "wy")
    in_specs = (
        P(walker),
        P(walker, None),
        P(walker),
        P(walker),
        P(None, "orb"),
        P("orb", None),
        P(walker, "orb", None),
    )
    out_specs = (P(walker + ("orb",)), P("orb", None))
    return jax.shard_map(body, mesh=split, in_specs=in_specs, out_specs=out_specs, check_vma=False)
```

```python
import jax
import jax.numpy as jnp
from jax import lax
from jax.sharding import Mesh, PartitionSpec as P


def _bits(axis):
    size = lax.axis_size(axis)
    count = size.bit_length() - 1
    assert 1 << count == size
    return size, count


def _exchange(x, axis, size, bit):
    pairs = [(i, i ^ (1 << bit)) for i in range(size)]
    return lax.ppermute(x, axis, pairs)


def _pick(x, which):
    return lax.dynamic_index_in_dim(x, which, 0, keepdims=False)


def reduce_scatter_bits(x, axis, order):
    size, _ = _bits(axis)
    me = lax.axis_index(axis)
    for bit in order:
        mine = (me >> bit) & 1
        keep = _pick(x, mine)
        send = _pick(x, 1 - mine)
        x = keep + _exchange(send, axis, size, bit)
    return x


def all_gather_bits(x, axis, order):
    size, _ = _bits(axis)
    me = lax.axis_index(axis)
    for bit in order:
        mine = (me >> bit) & 1
        other = _exchange(x, axis, size, bit)
        x = jnp.where(mine == 0, jnp.stack([x, other]), jnp.stack([other, x]))
    return x


def all_reduce_bits(x, axis):
    size, count = _bits(axis)
    tail = x.shape
    rows = tail[0] >> count
    parts = x.reshape((2,) * count + (rows,) + tail[1:])
    order = list(range(count))
    reduced = reduce_scatter_bits(parts, axis, order)
    return all_gather_bits(reduced, axis, order[::-1]).reshape(tail)


def all_reduce_walker(x, rider):
    me = lax.axis_index("wy")
    halves = x.reshape((2, x.shape[0] // 2) + x.shape[1:])
    keep = _pick(halves, me)
    half = keep + lax.ppermute(_pick(halves, 1 - me), "wy", [(0, 1), (1, 0)])
    half, rider = lax.optimization_barrier((half, rider))
    reduced = reduce_scatter_by_all_to_all(half, "zb")
    reduced = reduce_scatter_by_all_to_all(reduced, "za").astype(jnp.bfloat16)
    near = gather_by_all_to_all(reduced, "za").reshape((-1,) + reduced.shape[1:])
    half = gather_by_all_to_all(near, "zb").reshape(half.shape)
    other = lax.ppermute(half, "wy", [(0, 1), (1, 0)])
    full = jnp.where(me == 0, jnp.stack([half, other]), jnp.stack([other, half]))
    return full.reshape(x.shape).astype(x.dtype), rider


def gather_by_all_to_all(x, axis):
    size = lax.axis_size(axis)
    copies = jnp.broadcast_to(x[None], (size,) + x.shape)
    return lax.all_to_all(copies, axis, 0, 0, tiled=True)


def reduce_scatter_by_all_to_all(x, axis):
    size = lax.axis_size(axis)
    parts = x.reshape((size, x.shape[0] // size) + x.shape[1:])
    return jnp.sum(lax.all_to_all(parts, axis, 0, 0, tiled=True), axis=0)


def body(tile_index, weights, electron, strength, spline_table, rotation, inverse):
    points = tile_index.shape[0]
    coeffs = weights.shape[1]
    tiles_count = spline_table.shape[0] // coeffs
    electrons = inverse.shape[2]
    _, orb_bits = _bits("orb")
    inverse_full = gather_by_all_to_all(inverse[0], "orb").reshape(-1, electrons)
    onehot = (tile_index[:, None] == jnp.arange(tiles_count, dtype=jnp.int32)[None, :]).astype(
        jnp.bfloat16
    )
    stencil_matrix = (onehot[:, :, None] * weights[:, None, :]).reshape(
        points, tiles_count * coeffs
    )
    orbital_values = jnp.dot(
        stencil_matrix, spline_table, preferred_element_type=jnp.float32
    ).astype(jnp.bfloat16)
    pick = (electron[:, None] == jnp.arange(electrons, dtype=jnp.int32)[None, :]).astype(
        jnp.bfloat16
    )
    columns = lax.dot_general(
        pick, inverse_full, (((1,), (1,)), ((), ())), preferred_element_type=jnp.float32
    )
    adjoint = (columns * strength[:, None]).astype(jnp.bfloat16)
    local_gradient = lax.dot_general(
        orbital_values, adjoint, (((0,), (0,)), ((), ())), preferred_element_type=jnp.float32
    )
    rotated_columns = lax.dot_general(
        columns.astype(jnp.bfloat16),
        rotation,
        (((1,), (1,)), ((), ())),
        preferred_element_type=jnp.float32,
    )
    partial_ratio = jnp.sum(orbital_values.astype(jnp.float32) * rotated_columns, axis=1)
    ratios = reduce_scatter_by_all_to_all(partial_ratio, "orb")
    gradient, ratios = all_reduce_walker(local_gradient, ratios)
    return (ratios, gradient)


def solution(mesh):
    sizes = dict(mesh.shape)
    z_size = sizes["walker"] // 2
    near = 4 if z_size % 4 == 0 else z_size
    split = Mesh(
        mesh.devices.reshape(z_size // near, near, 2, sizes["orb"]), ("za", "zb", "wy", "orb")
    )
    walker = ("za", "zb", "wy")
    in_specs = (
        P(walker),
        P(walker, None),
        P(walker),
        P(walker),
        P(None, "orb"),
        P("orb", None),
        P(walker, "orb", None),
    )
    out_specs = (P(walker + ("orb",)), P("orb", None))
    return jax.shard_map(body, mesh=split, in_specs=in_specs, out_specs=out_specs, check_vma=False)
```

```python
import jax
import jax.numpy as jnp
from jax import lax
from jax.sharding import Mesh, PartitionSpec as P


def _bits(axis):
    size = lax.axis_size(axis)
    count = size.bit_length() - 1
    assert 1 << count == size
    return size, count


def _exchange(x, axis, size, bit):
    pairs = [(i, i ^ (1 << bit)) for i in range(size)]
    return lax.ppermute(x, axis, pairs)


def _pick(x, which):
    return lax.dynamic_index_in_dim(x, which, 0, keepdims=False)


def reduce_scatter_bits(x, axis, order):
    size, _ = _bits(axis)
    me = lax.axis_index(axis)
    for bit in order:
        mine = (me >> bit) & 1
        keep = _pick(x, mine)
        send = _pick(x, 1 - mine)
        x = keep + _exchange(send, axis, size, bit)
    return x


def all_gather_bits(x, axis, order):
    size, _ = _bits(axis)
    me = lax.axis_index(axis)
    for bit in order:
        mine = (me >> bit) & 1
        other = _exchange(x, axis, size, bit)
        x = jnp.where(mine == 0, jnp.stack([x, other]), jnp.stack([other, x]))
    return x


def all_reduce_bits(x, axis):
    size, count = _bits(axis)
    tail = x.shape
    rows = tail[0] >> count
    parts = x.reshape((2,) * count + (rows,) + tail[1:])
    order = list(range(count))
    reduced = reduce_scatter_bits(parts, axis, order)
    return all_gather_bits(reduced, axis, order[::-1]).reshape(tail)


def all_reduce_walker(x, rider):
    me = lax.axis_index("wy")
    halves = x.reshape((2, x.shape[0] // 2) + x.shape[1:])
    keep = _pick(halves, me)
    half = keep + lax.ppermute(_pick(halves, 1 - me), "wy", [(0, 1), (1, 0)])
    half, rider = lax.optimization_barrier((half, rider))
    reduced = reduce_scatter_by_all_to_all(half, "wz").astype(jnp.bfloat16)
    half = gather_by_all_to_all(reduced, "wz").reshape(half.shape)
    other = lax.ppermute(half, "wy", [(0, 1), (1, 0)])
    full = jnp.where(me == 0, jnp.stack([half, other]), jnp.stack([other, half]))
    return full.reshape(x.shape).astype(x.dtype), rider


def gather_by_all_to_all(x, axis):
    size = lax.axis_size(axis)
    copies = jnp.broadcast_to(x[None], (size,) + x.shape)
    return lax.all_to_all(copies, axis, 0, 0, tiled=True)


def reduce_scatter_by_all_to_all(x, axis):
    size = lax.axis_size(axis)
    parts = x.reshape((size, x.shape[0] // size) + x.shape[1:])
    return jnp.sum(lax.all_to_all(parts, axis, 0, 0, tiled=True), axis=0)


def body(tile_index, weights, electron, strength, spline_table, rotation, inverse):
    points = tile_index.shape[0]
    coeffs = weights.shape[1]
    tiles_count = spline_table.shape[0] // coeffs
    electrons = inverse.shape[2]
    own_core = gather_by_all_to_all(inverse[0], "oq")
    core = lax.axis_index("oc")
    other_core = lax.ppermute(own_core, "oc", [(0, 1), (1, 0)])
    pair = jnp.where(core == 0, jnp.stack([own_core, other_core], 1), jnp.stack([other_core, own_core], 1))
    inverse_full = pair.reshape(-1, electrons)
    onehot = (tile_index[:, None] == jnp.arange(tiles_count, dtype=jnp.int32)[None, :]).astype(
        jnp.bfloat16
    )
    stencil_matrix = (onehot[:, :, None] * weights[:, None, :]).reshape(
        points, tiles_count * coeffs
    )
    orbital_values = jnp.dot(
        stencil_matrix, spline_table, preferred_element_type=jnp.float32
    ).astype(jnp.bfloat16)
    pick = (electron[:, None] == jnp.arange(electrons, dtype=jnp.int32)[None, :]).astype(
        jnp.bfloat16
    )
    columns = lax.dot_general(
        pick, inverse_full, (((1,), (1,)), ((), ())), preferred_element_type=jnp.float32
    )
    adjoint = (columns * strength[:, None]).astype(jnp.bfloat16)
    local_gradient = lax.dot_general(
        orbital_values, adjoint, (((0,), (0,)), ((), ())), preferred_element_type=jnp.float32
    )
    rotated_columns = lax.dot_general(
        columns.astype(jnp.bfloat16),
        rotation,
        (((1,), (1,)), ((), ())),
        preferred_element_type=jnp.float32,
    )
    partial_ratio = jnp.sum(orbital_values.astype(jnp.float32) * rotated_columns, axis=1)
    ratios = reduce_scatter_by_all_to_all(partial_ratio, ("oq", "oc"))
    gradient, ratios = all_reduce_walker(local_gradient, ratios)
    return (ratios, gradient)


def solution(mesh):
    sizes = dict(mesh.shape)
    split = Mesh(
        mesh.devices.reshape(sizes["walker"] // 2, 2, sizes["orb"] // 2, 2),
        ("wz", "wy", "oq", "oc"),
    )
    walker = ("wz", "wy")
    orb = ("oq", "oc")
    in_specs = (
        P(walker),
        P(walker, None),
        P(walker),
        P(walker),
        P(None, orb),
        P(orb, None),
        P(walker, orb, None),
    )
    out_specs = (P(walker + orb), P(orb, None))
    return jax.shard_map(body, mesh=split, in_specs=in_specs, out_specs=out_specs, check_vma=False)
```

```python
import jax
import jax.numpy as jnp
from jax import lax
from jax.sharding import Mesh, PartitionSpec as P


def _bits(axis):
    size = lax.axis_size(axis)
    count = size.bit_length() - 1
    assert 1 << count == size
    return size, count


def _exchange(x, axis, size, bit):
    pairs = [(i, i ^ (1 << bit)) for i in range(size)]
    return lax.ppermute(x, axis, pairs)


def _pick(x, which):
    return lax.dynamic_index_in_dim(x, which, 0, keepdims=False)


def reduce_scatter_bits(x, axis, order):
    size, _ = _bits(axis)
    me = lax.axis_index(axis)
    for bit in order:
        mine = (me >> bit) & 1
        keep = _pick(x, mine)
        send = _pick(x, 1 - mine)
        x = keep + _exchange(send, axis, size, bit)
    return x


def all_gather_bits(x, axis, order):
    size, _ = _bits(axis)
    me = lax.axis_index(axis)
    for bit in order:
        mine = (me >> bit) & 1
        other = _exchange(x, axis, size, bit)
        x = jnp.where(mine == 0, jnp.stack([x, other]), jnp.stack([other, x]))
    return x


def all_reduce_bits(x, axis):
    size, count = _bits(axis)
    tail = x.shape
    rows = tail[0] >> count
    parts = x.reshape((2,) * count + (rows,) + tail[1:])
    order = list(range(count))
    reduced = reduce_scatter_bits(parts, axis, order)
    return all_gather_bits(reduced, axis, order[::-1]).reshape(tail)


def all_reduce_walker(x, rider):
    me = lax.axis_index("wy")
    halves = x.reshape((2, x.shape[0] // 2) + x.shape[1:])
    keep = _pick(halves, me)
    half = keep + lax.ppermute(_pick(halves, 1 - me), "wy", [(0, 1), (1, 0)])
    half, rider = lax.optimization_barrier((half, rider))
    reduced = reduce_scatter_by_all_to_all(half, "wz").astype(jnp.bfloat16)
    half = gather_by_all_to_all(reduced, "wz").reshape(half.shape)
    other = lax.ppermute(half, "wy", [(0, 1), (1, 0)])
    full = jnp.where(me == 0, jnp.stack([half, other]), jnp.stack([other, half]))
    return full.reshape(x.shape).astype(x.dtype), rider


def gather_by_all_to_all(x, axis):
    size = lax.axis_size(axis)
    copies = jnp.broadcast_to(x[None], (size,) + x.shape)
    return lax.all_to_all(copies, axis, 0, 0, tiled=True)


def reduce_scatter_by_all_to_all(x, axis):
    size = lax.axis_size(axis)
    parts = x.reshape((size, x.shape[0] // size) + x.shape[1:])
    return jnp.sum(lax.all_to_all(parts, axis, 0, 0, tiled=True), axis=0)


def body(tile_index, weights, electron, strength, spline_table, rotation, inverse):
    points = tile_index.shape[0]
    coeffs = weights.shape[1]
    tiles_count = spline_table.shape[0] // coeffs
    electrons = inverse.shape[2]
    onehot = (tile_index[:, None] == jnp.arange(tiles_count, dtype=jnp.int32)[None, :]).astype(
        jnp.bfloat16
    )
    stencil_matrix = (onehot[:, :, None] * weights[:, None, :]).reshape(
        points, tiles_count * coeffs
    )
    orbital_values = jnp.dot(
        stencil_matrix, spline_table, preferred_element_type=jnp.float32
    ).astype(jnp.bfloat16)
    own_core = gather_by_all_to_all(inverse[0], "oq")
    orbital_values, own_core = lax.optimization_barrier((orbital_values, own_core))
    core = lax.axis_index("oc")
    other_core = lax.ppermute(own_core, "oc", [(0, 1), (1, 0)])
    pair = jnp.where(core == 0, jnp.stack([own_core, other_core], 1), jnp.stack([other_core, own_core], 1))
    inverse_full = pair.reshape(-1, electrons)
    pick = (electron[:, None] == jnp.arange(electrons, dtype=jnp.int32)[None, :]).astype(
        jnp.bfloat16
    )
    columns = lax.dot_general(
        pick, inverse_full, (((1,), (1,)), ((), ())), preferred_element_type=jnp.float32
    )
    adjoint = (columns * strength[:, None]).astype(jnp.bfloat16)
    local_gradient = lax.dot_general(
        orbital_values, adjoint, (((0,), (0,)), ((), ())), preferred_element_type=jnp.float32
    )
    rotated_columns = lax.dot_general(
        columns.astype(jnp.bfloat16),
        rotation,
        (((1,), (1,)), ((), ())),
        preferred_element_type=jnp.float32,
    )
    partial_ratio = jnp.sum(orbital_values.astype(jnp.float32) * rotated_columns, axis=1)
    ratios = reduce_scatter_by_all_to_all(partial_ratio, ("oq", "oc"))
    gradient, ratios = all_reduce_walker(local_gradient, ratios)
    return (ratios, gradient)


def solution(mesh):
    sizes = dict(mesh.shape)
    split = Mesh(
        mesh.devices.reshape(sizes["walker"] // 2, 2, sizes["orb"] // 2, 2),
        ("wz", "wy", "oq", "oc"),
    )
    walker = ("wz", "wy")
    orb = ("oq", "oc")
    in_specs = (
        P(walker),
        P(walker, None),
        P(walker),
        P(walker),
        P(None, orb),
        P(orb, None),
        P(walker, orb, None),
    )
    out_specs = (P(walker + orb), P(orb, None))
    return jax.shard_map(body, mesh=split, in_specs=in_specs, out_specs=out_specs, check_vma=False)
```

```python
import jax
import jax.numpy as jnp
from jax import lax
from jax.sharding import Mesh, PartitionSpec as P


def _bits(axis):
    size = lax.axis_size(axis)
    count = size.bit_length() - 1
    assert 1 << count == size
    return size, count


def _exchange(x, axis, size, bit):
    pairs = [(i, i ^ (1 << bit)) for i in range(size)]
    return lax.ppermute(x, axis, pairs)


def _pick(x, which):
    return lax.dynamic_index_in_dim(x, which, 0, keepdims=False)


def reduce_scatter_bits(x, axis, order):
    size, _ = _bits(axis)
    me = lax.axis_index(axis)
    for bit in order:
        mine = (me >> bit) & 1
        keep = _pick(x, mine)
        send = _pick(x, 1 - mine)
        x = keep + _exchange(send, axis, size, bit)
    return x


def all_gather_bits(x, axis, order):
    size, _ = _bits(axis)
    me = lax.axis_index(axis)
    for bit in order:
        mine = (me >> bit) & 1
        other = _exchange(x, axis, size, bit)
        x = jnp.where(mine == 0, jnp.stack([x, other]), jnp.stack([other, x]))
    return x


def all_reduce_bits(x, axis):
    size, count = _bits(axis)
    tail = x.shape
    rows = tail[0] >> count
    parts = x.reshape((2,) * count + (rows,) + tail[1:])
    order = list(range(count))
    reduced = reduce_scatter_bits(parts, axis, order)
    return all_gather_bits(reduced, axis, order[::-1]).reshape(tail)


def all_reduce_walker(x, rider):
    me = lax.axis_index("wy")
    halves = x.reshape((2, x.shape[0] // 2) + x.shape[1:])
    keep = _pick(halves, me)
    half = keep + lax.ppermute(_pick(halves, 1 - me), "wy", [(0, 1), (1, 0)])
    half, rider = lax.optimization_barrier((half, rider))
    reduced = reduce_scatter_by_all_to_all(half, "wz").astype(jnp.bfloat16)
    half = gather_by_all_to_all(reduced, "wz").reshape(half.shape)
    other = lax.ppermute(half, "wy", [(0, 1), (1, 0)])
    full = jnp.where(me == 0, jnp.stack([half, other]), jnp.stack([other, half]))
    return full.reshape(x.shape).astype(x.dtype), rider


def gather_by_all_to_all(x, axis):
    size = lax.axis_size(axis)
    copies = jnp.broadcast_to(x[None], (size,) + x.shape)
    return lax.all_to_all(copies, axis, 0, 0, tiled=True)


def reduce_scatter_by_all_to_all(x, axis):
    size = lax.axis_size(axis)
    parts = x.reshape((size, x.shape[0] // size) + x.shape[1:])
    return jnp.sum(lax.all_to_all(parts, axis, 0, 0, tiled=True), axis=0)


def body(tile_index, weights, electron, strength, spline_table, rotation, inverse):
    points = tile_index.shape[0]
    coeffs = weights.shape[1]
    tiles_count = spline_table.shape[0] // coeffs
    electrons = inverse.shape[2]
    onehot = (tile_index[:, None] == jnp.arange(tiles_count, dtype=jnp.int32)[None, :]).astype(
        jnp.bfloat16
    )
    stencil_matrix = (onehot[:, :, None] * weights[:, None, :]).reshape(
        points, tiles_count * coeffs
    )
    orbital_values = jnp.dot(
        stencil_matrix, spline_table, preferred_element_type=jnp.float32
    ).astype(jnp.bfloat16)
    own_core = gather_by_all_to_all(inverse[0], "oq")
    orbital_values, own_core = lax.optimization_barrier((orbital_values, own_core))
    core = lax.axis_index("oc")
    other_core = lax.ppermute(own_core, "oc", [(0, 1), (1, 0)])
    pick = (electron[:, None] == jnp.arange(electrons, dtype=jnp.int32)[None, :]).astype(
        jnp.bfloat16
    )
    rows_per_block = inverse.shape[1]
    blocks = own_core.shape[0]
    rotation_blocks = rotation.reshape(rotation.shape[0], blocks, 2, rows_per_block)

    def half_terms(half_inverse, position):
        columns = lax.dot_general(
            pick,
            half_inverse.reshape(-1, electrons),
            (((1,), (1,)), ((), ())),
            preferred_element_type=jnp.float32,
        )
        adjoint = (columns * strength[:, None]).astype(jnp.bfloat16)
        gradient_half = lax.dot_general(
            orbital_values, adjoint, (((0,), (0,)), ((), ())), preferred_element_type=jnp.float32
        )
        rotation_half = lax.dynamic_index_in_dim(rotation_blocks, position, 2, keepdims=False)
        rotated_half = lax.dot_general(
            columns.astype(jnp.bfloat16),
            rotation_half.reshape(rotation.shape[0], -1),
            (((1,), (1,)), ((), ())),
            preferred_element_type=jnp.float32,
        )
        return gradient_half.reshape(-1, blocks, rows_per_block), rotated_half

    own_gradient, own_rotated = half_terms(own_core, core)
    other_gradient, other_rotated = half_terms(other_core, 1 - core)
    rotated_columns = own_rotated + other_rotated
    partial_ratio = jnp.sum(orbital_values.astype(jnp.float32) * rotated_columns, axis=1)
    ratios = reduce_scatter_by_all_to_all(partial_ratio, ("oq", "oc"))
    local_gradient = jnp.where(
        core == 0,
        jnp.stack([own_gradient, other_gradient], 2),
        jnp.stack([other_gradient, own_gradient], 2),
    ).reshape(orbital_values.shape[1], -1)
    gradient, ratios = all_reduce_walker(local_gradient, ratios)
    return (ratios, gradient)


def solution(mesh):
    sizes = dict(mesh.shape)
    split = Mesh(
        mesh.devices.reshape(sizes["walker"] // 2, 2, sizes["orb"] // 2, 2),
        ("wz", "wy", "oq", "oc"),
    )
    walker = ("wz", "wy")
    orb = ("oq", "oc")
    in_specs = (
        P(walker),
        P(walker, None),
        P(walker),
        P(walker),
        P(None, orb),
        P(orb, None),
        P(walker, orb, None),
    )
    out_specs = (P(walker + orb), P(orb, None))
    return jax.shard_map(body, mesh=split, in_specs=in_specs, out_specs=out_specs, check_vma=False)
```

```python
import jax
import jax.numpy as jnp
from jax import lax
from jax.sharding import Mesh, PartitionSpec as P


def _bits(axis):
    size = lax.axis_size(axis)
    count = size.bit_length() - 1
    assert 1 << count == size
    return size, count


def _exchange(x, axis, size, bit):
    pairs = [(i, i ^ (1 << bit)) for i in range(size)]
    return lax.ppermute(x, axis, pairs)


def _pick(x, which):
    return lax.dynamic_index_in_dim(x, which, 0, keepdims=False)


def reduce_scatter_bits(x, axis, order):
    size, _ = _bits(axis)
    me = lax.axis_index(axis)
    for bit in order:
        mine = (me >> bit) & 1
        keep = _pick(x, mine)
        send = _pick(x, 1 - mine)
        x = keep + _exchange(send, axis, size, bit)
    return x


def all_gather_bits(x, axis, order):
    size, _ = _bits(axis)
    me = lax.axis_index(axis)
    for bit in order:
        mine = (me >> bit) & 1
        other = _exchange(x, axis, size, bit)
        x = jnp.where(mine == 0, jnp.stack([x, other]), jnp.stack([other, x]))
    return x


def all_reduce_bits(x, axis):
    size, count = _bits(axis)
    tail = x.shape
    rows = tail[0] >> count
    parts = x.reshape((2,) * count + (rows,) + tail[1:])
    order = list(range(count))
    reduced = reduce_scatter_bits(parts, axis, order)
    return all_gather_bits(reduced, axis, order[::-1]).reshape(tail)


def all_reduce_walker(x, rider):
    me = lax.axis_index("wy")
    halves = x.reshape((2, x.shape[0] // 2) + x.shape[1:])
    keep = _pick(halves, me)
    half = keep + lax.ppermute(_pick(halves, 1 - me), "wy", [(0, 1), (1, 0)])
    half, rider = lax.optimization_barrier((half, rider))
    reduced = reduce_scatter_by_all_to_all(half, "wz").astype(jnp.bfloat16)
    half = gather_by_all_to_all(reduced, "wz").reshape(half.shape)
    other = lax.ppermute(half, "wy", [(0, 1), (1, 0)])
    full = jnp.where(me == 0, jnp.stack([half, other]), jnp.stack([other, half]))
    return full.reshape(x.shape).astype(x.dtype), rider


def gather_by_all_to_all(x, axis):
    size = lax.axis_size(axis)
    copies = jnp.broadcast_to(x[None], (size,) + x.shape)
    return lax.all_to_all(copies, axis, 0, 0, tiled=True)


def reduce_scatter_by_all_to_all(x, axis):
    size = lax.axis_size(axis)
    parts = x.reshape((size, x.shape[0] // size) + x.shape[1:])
    return jnp.sum(lax.all_to_all(parts, axis, 0, 0, tiled=True), axis=0)


def body(tile_index, weights, electron, strength, spline_table, rotation, inverse):
    points = tile_index.shape[0]
    coeffs = weights.shape[1]
    tiles_count = spline_table.shape[0] // coeffs
    electrons = inverse.shape[2]
    onehot = (tile_index[:, None] == jnp.arange(tiles_count, dtype=jnp.int32)[None, :]).astype(
        jnp.bfloat16
    )
    stencil_matrix = (onehot[:, :, None] * weights[:, None, :]).reshape(
        points, tiles_count * coeffs
    )
    orbital_values = jnp.dot(
        stencil_matrix, spline_table, preferred_element_type=jnp.float32
    ).astype(jnp.bfloat16)
    own_core = gather_by_all_to_all(inverse[0], "oq")
    orbital_values, own_core = lax.optimization_barrier((orbital_values, own_core))
    core = lax.axis_index("oc")
    other_core = lax.ppermute(own_core, "oc", [(0, 1), (1, 0)])
    pair = jnp.where(core == 0, jnp.stack([own_core, other_core], 1), jnp.stack([other_core, own_core], 1))
    inverse_full = pair.reshape(-1, electrons)
    pick = (electron[:, None] == jnp.arange(electrons, dtype=jnp.int32)[None, :]).astype(
        jnp.bfloat16
    )
    columns = lax.dot_general(
        pick, inverse_full, (((1,), (1,)), ((), ())), preferred_element_type=jnp.float32
    )
    adjoint = (columns * strength[:, None]).astype(jnp.bfloat16)
    local_gradient = lax.dot_general(
        orbital_values, adjoint, (((0,), (0,)), ((), ())), preferred_element_type=jnp.float32
    )
    rotated_columns = lax.dot_general(
        columns.astype(jnp.bfloat16),
        rotation,
        (((1,), (1,)), ((), ())),
        preferred_element_type=jnp.float32,
    )
    partial_ratio = jnp.sum(orbital_values.astype(jnp.float32) * rotated_columns, axis=1)
    ratios = reduce_scatter_by_all_to_all(partial_ratio, ("oq", "oc"))
    left, right = jnp.split(local_gradient, 2, axis=1)
    left, ratios = all_reduce_walker(left, ratios)
    right, _ = all_reduce_walker(right, right[:1, :1])
    gradient = jnp.concatenate([left, right], axis=1)
    return (ratios, gradient)


def solution(mesh):
    sizes = dict(mesh.shape)
    split = Mesh(
        mesh.devices.reshape(sizes["walker"] // 2, 2, sizes["orb"] // 2, 2),
        ("wz", "wy", "oq", "oc"),
    )
    walker = ("wz", "wy")
    orb = ("oq", "oc")
    in_specs = (
        P(walker),
        P(walker, None),
        P(walker),
        P(walker),
        P(None, orb),
        P(orb, None),
        P(walker, orb, None),
    )
    out_specs = (P(walker + orb), P(orb, None))
    return jax.shard_map(body, mesh=split, in_specs=in_specs, out_specs=out_specs, check_vma=False)
```

```python
import jax
import jax.numpy as jnp
from jax import lax
from jax.sharding import Mesh, PartitionSpec as P


def _bits(axis):
    size = lax.axis_size(axis)
    count = size.bit_length() - 1
    assert 1 << count == size
    return size, count


def _exchange(x, axis, size, bit):
    pairs = [(i, i ^ (1 << bit)) for i in range(size)]
    return lax.ppermute(x, axis, pairs)


def _pick(x, which):
    return lax.dynamic_index_in_dim(x, which, 0, keepdims=False)


def reduce_scatter_bits(x, axis, order):
    size, _ = _bits(axis)
    me = lax.axis_index(axis)
    for bit in order:
        mine = (me >> bit) & 1
        keep = _pick(x, mine)
        send = _pick(x, 1 - mine)
        x = keep + _exchange(send, axis, size, bit)
    return x


def all_gather_bits(x, axis, order):
    size, _ = _bits(axis)
    me = lax.axis_index(axis)
    for bit in order:
        mine = (me >> bit) & 1
        other = _exchange(x, axis, size, bit)
        x = jnp.where(mine == 0, jnp.stack([x, other]), jnp.stack([other, x]))
    return x


def all_reduce_bits(x, axis):
    size, count = _bits(axis)
    tail = x.shape
    rows = tail[0] >> count
    parts = x.reshape((2,) * count + (rows,) + tail[1:])
    order = list(range(count))
    reduced = reduce_scatter_bits(parts, axis, order)
    return all_gather_bits(reduced, axis, order[::-1]).reshape(tail)


def all_reduce_walker(x, rider):
    me = lax.axis_index("wy")
    halves = x.reshape((2, x.shape[0] // 2) + x.shape[1:])
    keep = _pick(halves, me)
    half = keep + lax.ppermute(_pick(halves, 1 - me), "wy", [(0, 1), (1, 0)])
    half, rider = lax.optimization_barrier((half, rider))
    reduced = reduce_scatter_by_all_to_all(half, "wz").astype(jnp.bfloat16)
    half = gather_by_all_to_all(reduced, "wz").reshape(half.shape)
    other = lax.ppermute(half, "wy", [(0, 1), (1, 0)])
    full = jnp.where(me == 0, jnp.stack([half, other]), jnp.stack([other, half]))
    return full.reshape(x.shape).astype(x.dtype), rider


def gather_by_all_to_all(x, axis):
    size = lax.axis_size(axis)
    copies = jnp.broadcast_to(x[None], (size,) + x.shape)
    return lax.all_to_all(copies, axis, 0, 0, tiled=True)


def reduce_scatter_by_all_to_all(x, axis):
    size = lax.axis_size(axis)
    parts = x.reshape((size, x.shape[0] // size) + x.shape[1:])
    return jnp.sum(lax.all_to_all(parts, axis, 0, 0, tiled=True), axis=0)


def body(tile_index, weights, electron, strength, spline_table, rotation, inverse):
    points = tile_index.shape[0]
    coeffs = weights.shape[1]
    tiles_count = spline_table.shape[0] // coeffs
    electrons = inverse.shape[2]
    onehot = (tile_index[:, None] == jnp.arange(tiles_count, dtype=jnp.int32)[None, :]).astype(
        jnp.bfloat16
    )
    stencil_matrix = (onehot[:, :, None] * weights[:, None, :]).reshape(
        points, tiles_count * coeffs
    )
    orbital_values = jnp.dot(
        stencil_matrix, spline_table, preferred_element_type=jnp.float32
    ).astype(jnp.bfloat16)
    own_core = gather_by_all_to_all(inverse[0], "oq")
    orbital_values, own_core = lax.optimization_barrier((orbital_values, own_core))
    core = lax.axis_index("oc")
    other_core = lax.ppermute(own_core, "oc", [(0, 1), (1, 0)])
    pair = jnp.where(core == 0, jnp.stack([own_core, other_core], 1), jnp.stack([other_core, own_core], 1))
    inverse_full = pair.reshape(-1, electrons)
    pick = (electron[:, None] == jnp.arange(electrons, dtype=jnp.int32)[None, :]).astype(
        jnp.bfloat16
    )
    columns = lax.dot_general(
        pick, inverse_full, (((1,), (1,)), ((), ())), preferred_element_type=jnp.float32
    )
    adjoint = (columns * strength[:, None]).astype(jnp.bfloat16)
    local_gradient = lax.dot_general(
        orbital_values, adjoint, (((0,), (0,)), ((), ())), preferred_element_type=jnp.float32
    )
    rotated_columns = lax.dot_general(
        columns.astype(jnp.bfloat16),
        rotation,
        (((1,), (1,)), ((), ())),
        preferred_element_type=jnp.float32,
    )
    partial_ratio = jnp.sum(orbital_values.astype(jnp.float32) * rotated_columns, axis=1)
    share = partial_ratio.shape[0] // lax.axis_size(("oq", "oc"))
    slot = lax.axis_index("oq") * lax.axis_size("oc") + lax.axis_index("oc")
    ratios = lax.dynamic_slice_in_dim(lax.psum(partial_ratio, ("oq", "oc")), slot * share, share)
    gradient, ratios = all_reduce_walker(local_gradient, ratios)
    return (ratios, gradient)


def solution(mesh):
    sizes = dict(mesh.shape)
    split = Mesh(
        mesh.devices.reshape(sizes["walker"] // 2, 2, sizes["orb"] // 2, 2),
        ("wz", "wy", "oq", "oc"),
    )
    walker = ("wz", "wy")
    orb = ("oq", "oc")
    in_specs = (
        P(walker),
        P(walker, None),
        P(walker),
        P(walker),
        P(None, orb),
        P(orb, None),
        P(walker, orb, None),
    )
    out_specs = (P(walker + orb), P(orb, None))
    return jax.shard_map(body, mesh=split, in_specs=in_specs, out_specs=out_specs, check_vma=False)
```

```python
import jax
import jax.numpy as jnp
from jax import lax
from jax.sharding import Mesh, PartitionSpec as P


def _bits(axis):
    size = lax.axis_size(axis)
    count = size.bit_length() - 1
    assert 1 << count == size
    return size, count


def _exchange(x, axis, size, bit):
    pairs = [(i, i ^ (1 << bit)) for i in range(size)]
    return lax.ppermute(x, axis, pairs)


def _pick(x, which):
    return lax.dynamic_index_in_dim(x, which, 0, keepdims=False)


def reduce_scatter_bits(x, axis, order):
    size, _ = _bits(axis)
    me = lax.axis_index(axis)
    for bit in order:
        mine = (me >> bit) & 1
        keep = _pick(x, mine)
        send = _pick(x, 1 - mine)
        x = keep + _exchange(send, axis, size, bit)
    return x


def all_gather_bits(x, axis, order):
    size, _ = _bits(axis)
    me = lax.axis_index(axis)
    for bit in order:
        mine = (me >> bit) & 1
        other = _exchange(x, axis, size, bit)
        x = jnp.where(mine == 0, jnp.stack([x, other]), jnp.stack([other, x]))
    return x


def all_reduce_bits(x, axis):
    size, count = _bits(axis)
    tail = x.shape
    rows = tail[0] >> count
    parts = x.reshape((2,) * count + (rows,) + tail[1:])
    order = list(range(count))
    reduced = reduce_scatter_bits(parts, axis, order)
    return all_gather_bits(reduced, axis, order[::-1]).reshape(tail)


def all_reduce_walker(x, rider):
    me = lax.axis_index("wy")
    halves = x.reshape((2, x.shape[0] // 2) + x.shape[1:])
    keep = _pick(halves, me)
    half = keep + lax.ppermute(_pick(halves, 1 - me), "wy", [(0, 1), (1, 0)])
    half, rider = lax.optimization_barrier((half, rider))
    reduced = reduce_scatter_by_all_to_all(half, "wz").astype(jnp.bfloat16)
    half = gather_by_all_to_all(reduced, "wz").reshape(half.shape)
    other = lax.ppermute(half, "wy", [(0, 1), (1, 0)])
    full = jnp.where(me == 0, jnp.stack([half, other]), jnp.stack([other, half]))
    return full.reshape(x.shape).astype(x.dtype), rider


def gather_by_all_to_all(x, axis):
    size = lax.axis_size(axis)
    copies = jnp.broadcast_to(x[None], (size,) + x.shape)
    return lax.all_to_all(copies, axis, 0, 0, tiled=True)


def reduce_scatter_by_all_to_all(x, axis):
    size = lax.axis_size(axis)
    parts = x.reshape((size, x.shape[0] // size) + x.shape[1:])
    return jnp.sum(lax.all_to_all(parts, axis, 0, 0, tiled=True), axis=0)


def body(tile_index, weights, electron, strength, spline_table, rotation, inverse):
    points = tile_index.shape[0]
    coeffs = weights.shape[1]
    tiles_count = spline_table.shape[0] // coeffs
    electrons = inverse.shape[2]
    onehot = (tile_index[:, None] == jnp.arange(tiles_count, dtype=jnp.int32)[None, :]).astype(
        jnp.bfloat16
    )
    stencil_matrix = (onehot[:, :, None] * weights[:, None, :]).reshape(
        points, tiles_count * coeffs
    )
    orbital_values = jnp.dot(
        stencil_matrix, spline_table, preferred_element_type=jnp.float32
    ).astype(jnp.bfloat16)
    own_core = gather_by_all_to_all(inverse[0], "oq")
    orbital_values, own_core = lax.optimization_barrier((orbital_values, own_core))
    core = lax.axis_index("oc")
    other_core = lax.ppermute(own_core, "oc", [(0, 1), (1, 0)])
    pair = jnp.zeros((own_core.shape[0], 2) + own_core.shape[1:], own_core.dtype)
    pair = lax.dynamic_update_index_in_dim(pair, own_core, core, 1)
    pair = lax.dynamic_update_index_in_dim(pair, other_core, 1 - core, 1)
    inverse_full = pair.reshape(-1, electrons)
    pick = (electron[:, None] == jnp.arange(electrons, dtype=jnp.int32)[None, :]).astype(
        jnp.bfloat16
    )
    columns = lax.dot_general(
        pick, inverse_full, (((1,), (1,)), ((), ())), preferred_element_type=jnp.float32
    )
    adjoint = (columns * strength[:, None]).astype(jnp.bfloat16)
    local_gradient = lax.dot_general(
        orbital_values, adjoint, (((0,), (0,)), ((), ())), preferred_element_type=jnp.float32
    )
    rotated_columns = lax.dot_general(
        columns.astype(jnp.bfloat16),
        rotation,
        (((1,), (1,)), ((), ())),
        preferred_element_type=jnp.float32,
    )
    partial_ratio = jnp.sum(orbital_values.astype(jnp.float32) * rotated_columns, axis=1)
    ratios = reduce_scatter_by_all_to_all(partial_ratio, ("oq", "oc"))
    gradient, ratios = all_reduce_walker(local_gradient, ratios)
    return (ratios, gradient)


def solution(mesh):
    sizes = dict(mesh.shape)
    split = Mesh(
        mesh.devices.reshape(sizes["walker"] // 2, 2, sizes["orb"] // 2, 2),
        ("wz", "wy", "oq", "oc"),
    )
    walker = ("wz", "wy")
    orb = ("oq", "oc")
    in_specs = (
        P(walker),
        P(walker, None),
        P(walker),
        P(walker),
        P(None, orb),
        P(orb, None),
        P(walker, orb, None),
    )
    out_specs = (P(walker + orb), P(orb, None))
    return jax.shard_map(body, mesh=split, in_specs=in_specs, out_specs=out_specs, check_vma=False)
```

```python
import jax
import jax.numpy as jnp
from jax import lax
from jax.sharding import Mesh, PartitionSpec as P


def _bits(axis):
    size = lax.axis_size(axis)
    count = size.bit_length() - 1
    assert 1 << count == size
    return size, count


def _exchange(x, axis, size, bit):
    pairs = [(i, i ^ (1 << bit)) for i in range(size)]
    return lax.ppermute(x, axis, pairs)


def _pick(x, which):
    return lax.dynamic_index_in_dim(x, which, 0, keepdims=False)


def reduce_scatter_bits(x, axis, order):
    size, _ = _bits(axis)
    me = lax.axis_index(axis)
    for bit in order:
        mine = (me >> bit) & 1
        keep = _pick(x, mine)
        send = _pick(x, 1 - mine)
        x = keep + _exchange(send, axis, size, bit)
    return x


def all_gather_bits(x, axis, order):
    size, _ = _bits(axis)
    me = lax.axis_index(axis)
    for bit in order:
        mine = (me >> bit) & 1
        other = _exchange(x, axis, size, bit)
        x = jnp.where(mine == 0, jnp.stack([x, other]), jnp.stack([other, x]))
    return x


def all_reduce_bits(x, axis):
    size, count = _bits(axis)
    tail = x.shape
    rows = tail[0] >> count
    parts = x.reshape((2,) * count + (rows,) + tail[1:])
    order = list(range(count))
    reduced = reduce_scatter_bits(parts, axis, order)
    return all_gather_bits(reduced, axis, order[::-1]).reshape(tail)


def all_reduce_walker(x, rider):
    me = lax.axis_index("wy")
    halves = x.reshape((2, x.shape[0] // 2) + x.shape[1:])
    keep = _pick(halves, me)
    half = keep + lax.ppermute(_pick(halves, 1 - me), "wy", [(0, 1), (1, 0)])
    half, rider = lax.optimization_barrier((half, rider))
    reduced = reduce_scatter_by_all_to_all(half, "wz").astype(jnp.bfloat16)
    half = gather_by_all_to_all(reduced, "wz").reshape(half.shape)
    other = lax.ppermute(half, "wy", [(0, 1), (1, 0)])
    full = jnp.zeros((2,) + half.shape, x.dtype)
    full = lax.dynamic_update_index_in_dim(full, half.astype(x.dtype), me, 0)
    full = lax.dynamic_update_index_in_dim(full, other.astype(x.dtype), 1 - me, 0)
    return full.reshape(x.shape), rider


def gather_by_all_to_all(x, axis):
    size = lax.axis_size(axis)
    copies = jnp.broadcast_to(x[None], (size,) + x.shape)
    return lax.all_to_all(copies, axis, 0, 0, tiled=True)


def reduce_scatter_by_all_to_all(x, axis):
    size = lax.axis_size(axis)
    parts = x.reshape((size, x.shape[0] // size) + x.shape[1:])
    return jnp.sum(lax.all_to_all(parts, axis, 0, 0, tiled=True), axis=0)


def body(tile_index, weights, electron, strength, spline_table, rotation, inverse):
    points = tile_index.shape[0]
    coeffs = weights.shape[1]
    tiles_count = spline_table.shape[0] // coeffs
    electrons = inverse.shape[2]
    onehot = (tile_index[:, None] == jnp.arange(tiles_count, dtype=jnp.int32)[None, :]).astype(
        jnp.bfloat16
    )
    stencil_matrix = (onehot[:, :, None] * weights[:, None, :]).reshape(
        points, tiles_count * coeffs
    )
    orbital_values = jnp.dot(
        stencil_matrix, spline_table, preferred_element_type=jnp.float32
    ).astype(jnp.bfloat16)
    own_core = gather_by_all_to_all(inverse[0], "oq")
    orbital_values, own_core = lax.optimization_barrier((orbital_values, own_core))
    core = lax.axis_index("oc")
    other_core = lax.ppermute(own_core, "oc", [(0, 1), (1, 0)])
    pair = jnp.zeros((own_core.shape[0], 2) + own_core.shape[1:], own_core.dtype)
    pair = lax.dynamic_update_index_in_dim(pair, own_core, core, 1)
    pair = lax.dynamic_update_index_in_dim(pair, other_core, 1 - core, 1)
    inverse_full = pair.reshape(-1, electrons)
    pick = (electron[:, None] == jnp.arange(electrons, dtype=jnp.int32)[None, :]).astype(
        jnp.bfloat16
    )
    columns = lax.dot_general(
        pick, inverse_full, (((1,), (1,)), ((), ())), preferred_element_type=jnp.float32
    )
    adjoint = (columns * strength[:, None]).astype(jnp.bfloat16)
    local_gradient = lax.dot_general(
        orbital_values, adjoint, (((0,), (0,)), ((), ())), preferred_element_type=jnp.float32
    )
    rotated_columns = lax.dot_general(
        columns.astype(jnp.bfloat16),
        rotation,
        (((1,), (1,)), ((), ())),
        preferred_element_type=jnp.float32,
    )
    partial_ratio = jnp.sum(orbital_values.astype(jnp.float32) * rotated_columns, axis=1)
    ratios = reduce_scatter_by_all_to_all(partial_ratio, ("oq", "oc"))
    gradient, ratios = all_reduce_walker(local_gradient, ratios)
    return (ratios, gradient)


def solution(mesh):
    sizes = dict(mesh.shape)
    split = Mesh(
        mesh.devices.reshape(sizes["walker"] // 2, 2, sizes["orb"] // 2, 2),
        ("wz", "wy", "oq", "oc"),
    )
    walker = ("wz", "wy")
    orb = ("oq", "oc")
    in_specs = (
        P(walker),
        P(walker, None),
        P(walker),
        P(walker),
        P(None, orb),
        P(orb, None),
        P(walker, orb, None),
    )
    out_specs = (P(walker + orb), P(orb, None))
    return jax.shard_map(body, mesh=split, in_specs=in_specs, out_specs=out_specs, check_vma=False)
```

```python
import jax
import jax.numpy as jnp
from jax import lax
from jax.sharding import Mesh, PartitionSpec as P


def _bits(axis):
    size = lax.axis_size(axis)
    count = size.bit_length() - 1
    assert 1 << count == size
    return size, count


def _exchange(x, axis, size, bit):
    pairs = [(i, i ^ (1 << bit)) for i in range(size)]
    return lax.ppermute(x, axis, pairs)


def _pick(x, which):
    return lax.dynamic_index_in_dim(x, which, 0, keepdims=False)


def reduce_scatter_bits(x, axis, order):
    size, _ = _bits(axis)
    me = lax.axis_index(axis)
    for bit in order:
        mine = (me >> bit) & 1
        keep = _pick(x, mine)
        send = _pick(x, 1 - mine)
        x = keep + _exchange(send, axis, size, bit)
    return x


def all_gather_bits(x, axis, order):
    size, _ = _bits(axis)
    me = lax.axis_index(axis)
    for bit in order:
        mine = (me >> bit) & 1
        other = _exchange(x, axis, size, bit)
        x = jnp.where(mine == 0, jnp.stack([x, other]), jnp.stack([other, x]))
    return x


def all_reduce_bits(x, axis):
    size, count = _bits(axis)
    tail = x.shape
    rows = tail[0] >> count
    parts = x.reshape((2,) * count + (rows,) + tail[1:])
    order = list(range(count))
    reduced = reduce_scatter_bits(parts, axis, order)
    return all_gather_bits(reduced, axis, order[::-1]).reshape(tail)


def all_reduce_walker(half_of, rider, shape):
    me = lax.axis_index("wy")
    sent = lax.ppermute(half_of(1 - me), "wy", [(0, 1), (1, 0)])
    half = half_of(me) + sent
    half, rider = lax.optimization_barrier((half, rider))
    reduced = reduce_scatter_by_all_to_all(half, "wz").astype(jnp.bfloat16)
    half = gather_by_all_to_all(reduced, "wz").reshape(half.shape)
    other = lax.ppermute(half, "wy", [(0, 1), (1, 0)])
    full = jnp.where(me == 0, jnp.stack([half, other]), jnp.stack([other, half]))
    return full.reshape(shape).astype(jnp.float32), rider


def gather_by_all_to_all(x, axis):
    size = lax.axis_size(axis)
    copies = jnp.broadcast_to(x[None], (size,) + x.shape)
    return lax.all_to_all(copies, axis, 0, 0, tiled=True)


def reduce_scatter_by_all_to_all(x, axis):
    size = lax.axis_size(axis)
    parts = x.reshape((size, x.shape[0] // size) + x.shape[1:])
    return jnp.sum(lax.all_to_all(parts, axis, 0, 0, tiled=True), axis=0)


def body(tile_index, weights, electron, strength, spline_table, rotation, inverse):
    points = tile_index.shape[0]
    coeffs = weights.shape[1]
    tiles_count = spline_table.shape[0] // coeffs
    electrons = inverse.shape[2]
    onehot = (tile_index[:, None] == jnp.arange(tiles_count, dtype=jnp.int32)[None, :]).astype(
        jnp.bfloat16
    )
    stencil_matrix = (onehot[:, :, None] * weights[:, None, :]).reshape(
        points, tiles_count * coeffs
    )
    orbital_values = jnp.dot(
        stencil_matrix, spline_table, preferred_element_type=jnp.float32
    ).astype(jnp.bfloat16)
    own_core = gather_by_all_to_all(inverse[0], "oq")
    orbital_values, own_core = lax.optimization_barrier((orbital_values, own_core))
    core = lax.axis_index("oc")
    other_core = lax.ppermute(own_core, "oc", [(0, 1), (1, 0)])
    pair = jnp.zeros((own_core.shape[0], 2) + own_core.shape[1:], own_core.dtype)
    pair = lax.dynamic_update_index_in_dim(pair, own_core, core, 1)
    pair = lax.dynamic_update_index_in_dim(pair, other_core, 1 - core, 1)
    inverse_full = pair.reshape(-1, electrons)
    pick = (electron[:, None] == jnp.arange(electrons, dtype=jnp.int32)[None, :]).astype(
        jnp.bfloat16
    )
    columns = lax.dot_general(
        pick, inverse_full, (((1,), (1,)), ((), ())), preferred_element_type=jnp.float32
    )
    adjoint = (columns * strength[:, None]).astype(jnp.bfloat16)
    half_rows = orbital_values.shape[1] // 2

    def gradient_half(which):
        values_half = lax.dynamic_slice_in_dim(orbital_values, which * half_rows, half_rows, 1)
        return lax.dot_general(
            values_half, adjoint, (((0,), (0,)), ((), ())), preferred_element_type=jnp.float32
        )

    rotated_columns = lax.dot_general(
        columns.astype(jnp.bfloat16),
        rotation,
        (((1,), (1,)), ((), ())),
        preferred_element_type=jnp.float32,
    )
    partial_ratio = jnp.sum(orbital_values.astype(jnp.float32) * rotated_columns, axis=1)
    ratios = reduce_scatter_by_all_to_all(partial_ratio, ("oq", "oc"))
    gradient, ratios = all_reduce_walker(
        gradient_half, ratios, (orbital_values.shape[1], adjoint.shape[1])
    )
    return (ratios, gradient)


def solution(mesh):
    sizes = dict(mesh.shape)
    split = Mesh(
        mesh.devices.reshape(sizes["walker"] // 2, 2, sizes["orb"] // 2, 2),
        ("wz", "wy", "oq", "oc"),
    )
    walker = ("wz", "wy")
    orb = ("oq", "oc")
    in_specs = (
        P(walker),
        P(walker, None),
        P(walker),
        P(walker),
        P(None, orb),
        P(orb, None),
        P(walker, orb, None),
    )
    out_specs = (P(walker + orb), P(orb, None))
    return jax.shard_map(body, mesh=split, in_specs=in_specs, out_specs=out_specs, check_vma=False)
```
